512 devices in a mesh: layer: 4 (over x), row: 8 (over y, core), col: 16 (over z).
Axes of the slice: x: 4, y: 4, z: 16, core: 2. Of those that a mesh axis runs over, the one named last changes fastest.
Arguments:
- density: bfloat16 [8192, 8192], P('row', 'col'), may hold values from -0.125 to 0.125
- hamiltonian: bfloat16 [8192, 8192], P('row', 'col'), may hold values from -6 to 6
- density_mask: int32 [128, 128], P('row', 'col'), may hold values from 0 to 1, as said below
- hamilton_mask: int32 [128, 128], P('row', 'col'), may hold values from 0 to 1, as said below
- filter_mask: int32 [128, 128], P('row', 'col'), may hold values from 0 to 1, as said below
Outputs:
- weighted: bfloat16 [8192, 8192], P('row', 'col')
The draws below stay inside these ranges and needn't reach their ends.
Inputs may be any that keep to these rules, and one draw needn't show every extreme that they name: `density_mask`: each entry is 0 or 1; diagonal blocks are 1. `hamilton_mask`: each entry is 0 or 1; diagonal blocks are 1. `filter_mask`: each entry is 0 or 1; diagonal blocks are 1.
All inputs are finite; a program needn't handle non-finite values.
Results may differ from the reference program's by a relative error of at most 0.005.
Values may be sent and summed in bfloat16 or wider, within the bound.
No kernel may reach another device: no remote copies, remote signals or barrier semaphores. Data moves between devices by JAX's collectives and lax.ppermute only.
A program may use at most 64 MiB of HBM per device.

```python
import jax
import jax.numpy as jnp

BS = 64
NB = 128
N = 8192


def block_pattern(key, keep):
    rows = jnp.arange(NB, dtype=jnp.int32)[:, None]
    cols = jnp.arange(NB, dtype=jnp.int32)[None, :]
    coins = jax.random.randint(key, (NB, NB), 0, 8)
    kept = (coins < keep) | (rows == cols)
    return kept.astype(jnp.int32)


def draw_density_mask(key, part):
    return block_pattern(jax.random.fold_in(key, 11), 5)


def draw_hamilton_mask(key, part):
    return block_pattern(jax.random.fold_in(key, 23), 5)


def draw_filter_mask(key, part):
    return block_pattern(jax.random.fold_in(key, 37), 6)


def block_scale(key, dims, split, low, high):
    def one(dim, blocks):
        heights = jax.random.uniform(jax.random.fold_in(jax.random.fold_in(key, 6), dim), (blocks,), jnp.float32, low / len(split), high / len(split))
        return jnp.repeat(jnp.exp(heights), dims[dim] // blocks).reshape((-1,) + (1,) * (len(dims) - dim - 1))

    factor_of = one(*split[0])
    for cut in split[1:]:
        factor_of = factor_of * one(*cut)
    return factor_of


def bell_draw(key, shape, scale, bound, cuts=(), kind=jnp.bfloat16):
    entries = jax.random.normal(key, shape, jnp.float32) * scale
    if len(cuts) > 0:
        entries = block_scale(key, shape, cuts, -0.22, 0.18) * entries
    return jnp.clip(entries, min=-bound, max=bound).astype(kind)


def setup_inputs(seed: int = 0) -> dict:
    key_of = jax.random.split(jax.random.key(seed), 6)
    return {
        "density": bell_draw(key_of[0], (N, N), (N // 4) ** -0.5, 0.125, ((0, 8), (1, 16))),
        "hamiltonian": bell_draw(key_of[1], (N, N), 1.0, 6.0, ((0, 8), (1, 16))),
        "density_mask": draw_density_mask(jax.random.fold_in(key_of[5], 71), 0),
        "hamilton_mask": draw_hamilton_mask(jax.random.fold_in(key_of[5], 71), 0),
        "filter_mask": draw_filter_mask(jax.random.fold_in(key_of[5], 71), 0),
    }


def expand_mask(mask_blocks):
    return jnp.repeat(jnp.repeat(mask_blocks, BS, axis=0), BS, axis=1).astype(jnp.bfloat16)


def reference(density, hamiltonian, density_mask, hamilton_mask, filter_mask):
    masked_p = density * expand_mask(density_mask)
    masked_h = hamiltonian * expand_mask(hamilton_mask)
    product = jnp.dot(masked_p, masked_h, preferred_element_type=jnp.float32).astype(jnp.bfloat16)
    product = product * expand_mask(filter_mask)
    weighted = jnp.dot(product, masked_p, preferred_element_type=jnp.float32)
    return weighted.astype(jnp.bfloat16)
```

```python
import jax
import jax.numpy as jnp
from jax import lax
from jax.sharding import PartitionSpec as P

BS = 64


def expand_mask(mask_blocks):
    return jnp.repeat(jnp.repeat(mask_blocks, BS, axis=0), BS, axis=1).astype(jnp.bfloat16)


def inner_rows(matrix, groups, width, layer_pos):
    pieces = []
    stride = matrix.shape[0] // groups
    for group in range(groups):
        offset = group * stride + layer_pos * width
        pieces.append(lax.dynamic_slice_in_dim(matrix, offset, width, 0))
    return jnp.concatenate(pieces, axis=0)


def ring_gather(block, axis, n):
    fwd = [(i, (i + 1) % n) for i in range(n)]
    bwd = [(i, (i - 1) % n) for i in range(n)]
    got = [None] * n
    got[0] = block
    a = block
    b = block
    for s in range(1, n // 2 + 1):
        a = lax.ppermute(a, axis, fwd)
        got[(n - s) % n] = a
        if s <= (n - 1) // 2:
            b = lax.ppermute(b, axis, bwd)
            got[s] = b
    return got


def rotated(blocks, axis, n, dim):
    me = lax.axis_index(axis)
    full = jnp.concatenate(blocks + blocks, axis=dim)
    size = blocks[0].shape[dim]
    return lax.dynamic_slice_in_dim(full, me * size, n * size, dim)


def local(density, hamiltonian, density_mask, hamilton_mask, filter_mask):
    layers = lax.axis_size("layer")
    layer_pos = lax.axis_index("layer")
    nrow = lax.axis_size("row")
    ncol = lax.axis_size("col")
    groups = ncol // nrow
    tile_rows, tile_cols = density.shape
    width = tile_cols // layers
    masked_p = density * expand_mask(density_mask)
    masked_h = hamiltonian * expand_mask(hamilton_mask)

    h_blocks = ring_gather(inner_rows(masked_h, groups, width, layer_pos), "row", nrow)
    p_blocks = ring_gather(lax.dynamic_slice_in_dim(masked_p, layer_pos * width, width, 1), "col", ncol)
    h_inner = jnp.concatenate(h_blocks, axis=0)
    row_me = lax.axis_index("row")
    h_inner = lax.dynamic_slice_in_dim(jnp.concatenate([h_inner, h_inner], 0), (nrow - row_me) % nrow * (groups * width), nrow * groups * width, 0)
    col_me = lax.axis_index("col")
    h_rot = lax.dynamic_slice_in_dim(jnp.concatenate([h_inner, h_inner], 0), col_me * width, ncol * width, 0)
    p_rot = jnp.concatenate(p_blocks, axis=1)
    partial_q = jnp.dot(p_rot, h_rot, preferred_element_type=jnp.float32)
    summed_q = lax.psum_scatter(partial_q, "layer", scatter_dimension=1, tiled=True)
    filter_share = lax.dynamic_slice_in_dim(filter_mask, layer_pos * (width // BS), width // BS, 1)
    product = summed_q.astype(jnp.bfloat16) * expand_mask(filter_share)

    pr_blocks = ring_gather(inner_rows(masked_p, groups, width, layer_pos), "row", nrow)
    p_inner = jnp.concatenate(pr_blocks, axis=0)
    p_inner = lax.dynamic_slice_in_dim(jnp.concatenate([p_inner, p_inner], 0), (nrow - row_me) % nrow * (groups * width), nrow * groups * width, 0)
    p_rows = lax.dynamic_slice_in_dim(jnp.concatenate([p_inner, p_inner], 0), col_me * width, ncol * width, 0)
    q_blocks = ring_gather(product, "col", ncol)
    q_rot = jnp.concatenate(q_blocks, axis=1)
    partial_w = jnp.dot(q_rot, p_rows, preferred_element_type=jnp.float32)
    weighted = lax.psum(partial_w, "layer").astype(jnp.bfloat16)
    return weighted


def solution(mesh):
    placed = (P("row", "col"), P("row", "col"), P("row", "col"), P("row", "col"), P("row", "col"))
    return jax.shard_map(
        local, mesh=mesh, in_specs=placed, out_specs=P("row", "col"), check_vma=False
    )
```

```python
import jax
import jax.numpy as jnp
from jax import lax
from jax.sharding import PartitionSpec as P

BS = 64


def expand_mask(mask_blocks):
    return jnp.repeat(jnp.repeat(mask_blocks, BS, axis=0), BS, axis=1).astype(jnp.bfloat16)


def inner_rows(matrix, groups, width, layer_pos):
    pieces = []
    stride = matrix.shape[0] // groups
    for group in range(groups):
        offset = group * stride + layer_pos * width
        pieces.append(lax.dynamic_slice_in_dim(matrix, offset, width, 0))
    return jnp.concatenate(pieces, axis=0)


def ring_gather(block, axis, n):
    fwd = [(i, (i + 1) % n) for i in range(n)]
    bwd = [(i, (i - 1) % n) for i in range(n)]
    got = [None] * n
    got[0] = block
    a = block
    b = block
    for s in range(1, n // 2 + 1):
        a = lax.ppermute(a, axis, fwd)
        got[(n - s) % n] = a
        if s <= (n - 1) // 2:
            b = lax.ppermute(b, axis, bwd)
            got[s] = b
    return got


def rotated(blocks, axis, n, dim):
    me = lax.axis_index(axis)
    full = jnp.concatenate(blocks + blocks, axis=dim)
    size = blocks[0].shape[dim]
    return lax.dynamic_slice_in_dim(full, me * size, n * size, dim)


def local(density, hamiltonian, density_mask, hamilton_mask, filter_mask):
    layers = lax.axis_size("layer")
    layer_pos = lax.axis_index("layer")
    nrow = lax.axis_size("row")
    ncol = lax.axis_size("col")
    groups = ncol // nrow
    tile_rows, tile_cols = density.shape
    width = tile_cols // layers
    masked_p = density * expand_mask(density_mask)
    masked_h = hamiltonian * expand_mask(hamilton_mask)

    h_blocks = ring_gather(inner_rows(masked_h, groups, width, layer_pos), "row", nrow)
    p_blocks = ring_gather(lax.dynamic_slice_in_dim(masked_p, layer_pos * width, width, 1), "col", ncol)
    h_inner = jnp.concatenate(h_blocks, axis=0)
    row_me = lax.axis_index("row")
    h_inner = lax.dynamic_slice_in_dim(jnp.concatenate([h_inner, h_inner], 0), (nrow - row_me) % nrow * (groups * width), nrow * groups * width, 0)
    col_me = lax.axis_index("col")
    h_rot = lax.dynamic_slice_in_dim(jnp.concatenate([h_inner, h_inner], 0), col_me * width, ncol * width, 0)
    p_rot = jnp.concatenate(p_blocks, axis=1)
    partial_q = jnp.dot(p_rot, h_rot, preferred_element_type=jnp.float32)
    summed_q = lax.dynamic_slice_in_dim(lax.psum(partial_q, "layer"), layer_pos * width, width, 1)
    filter_share = lax.dynamic_slice_in_dim(filter_mask, layer_pos * (width // BS), width // BS, 1)
    product = summed_q.astype(jnp.bfloat16) * expand_mask(filter_share)

    pr_blocks = ring_gather(inner_rows(masked_p, groups, width, layer_pos), "row", nrow)
    p_inner = jnp.concatenate(pr_blocks, axis=0)
    p_inner = lax.dynamic_slice_in_dim(jnp.concatenate([p_inner, p_inner], 0), (nrow - row_me) % nrow * (groups * width), nrow * groups * width, 0)
    p_rows = lax.dynamic_slice_in_dim(jnp.concatenate([p_inner, p_inner], 0), col_me * width, ncol * width, 0)
    q_blocks = ring_gather(product, "col", ncol)
    q_rot = jnp.concatenate(q_blocks, axis=1)
    partial_w = jnp.dot(q_rot, p_rows, preferred_element_type=jnp.float32)
    weighted = lax.psum(partial_w, "layer").astype(jnp.bfloat16)
    return weighted


def solution(mesh):
    placed = (P("row", "col"), P("row", "col"), P("row", "col"), P("row", "col"), P("row", "col"))
    return jax.shard_map(
        local, mesh=mesh, in_specs=placed, out_specs=P("row", "col"), check_vma=False
    )
```

```python
import jax
import jax.numpy as jnp
from jax import lax
from jax.sharding import PartitionSpec as P

BS = 64


def expand_mask(mask_blocks):
    return jnp.repeat(jnp.repeat(mask_blocks, BS, axis=0), BS, axis=1).astype(jnp.bfloat16)


def inner_rows(matrix, groups, width, layer_pos):
    pieces = []
    stride = matrix.shape[0] // groups
    for group in range(groups):
        offset = group * stride + layer_pos * width
        pieces.append(lax.dynamic_slice_in_dim(matrix, offset, width, 0))
    return jnp.concatenate(pieces, axis=0)


def ring_gather(block, axis, n):
    fwd = [(i, (i + 1) % n) for i in range(n)]
    bwd = [(i, (i - 1) % n) for i in range(n)]
    got = [None] * n
    got[0] = block
    a = block
    b = block
    for s in range(1, n // 2 + 1):
        a = lax.ppermute(a, axis, fwd)
        got[(n - s) % n] = a
        if s <= (n - 1) // 2:
            b = lax.ppermute(b, axis, bwd)
            got[s] = b
    return got


def rotated(blocks, axis, n, dim):
    me = lax.axis_index(axis)
    full = jnp.concatenate(blocks + blocks, axis=dim)
    size = blocks[0].shape[dim]
    return lax.dynamic_slice_in_dim(full, me * size, n * size, dim)


def ring_dot(blocks, rows, width):
    n = len(blocks)
    order = [0]
    for s in range(1, n // 2 + 1):
        order.append((n - s) % n)
        if s <= (n - 1) // 2:
            order.append(s)
    acc = None
    for k in order:
        part = jnp.dot(blocks[k], rows[k * width:(k + 1) * width], preferred_element_type=jnp.float32)
        acc = part if acc is None else acc + part
    return acc


def local(density, hamiltonian, density_mask, hamilton_mask, filter_mask):
    layers = lax.axis_size("layer")
    layer_pos = lax.axis_index("layer")
    nrow = lax.axis_size("row")
    ncol = lax.axis_size("col")
    groups = ncol // nrow
    tile_rows, tile_cols = density.shape
    width = tile_cols // layers
    masked_p = density * expand_mask(density_mask)
    masked_h = hamiltonian * expand_mask(hamilton_mask)

    h_blocks = ring_gather(inner_rows(masked_h, groups, width, layer_pos), "row", nrow)
    p_blocks = ring_gather(lax.dynamic_slice_in_dim(masked_p, layer_pos * width, width, 1), "col", ncol)
    h_inner = jnp.concatenate(h_blocks, axis=0)
    row_me = lax.axis_index("row")
    h_inner = lax.dynamic_slice_in_dim(jnp.concatenate([h_inner, h_inner], 0), (nrow - row_me) % nrow * (groups * width), nrow * groups * width, 0)
    col_me = lax.axis_index("col")
    h_rot = lax.dynamic_slice_in_dim(jnp.concatenate([h_inner, h_inner], 0), col_me * width, ncol * width, 0)
    partial_q = ring_dot(p_blocks, h_rot, width)
    summed_q = lax.psum_scatter(partial_q, "layer", scatter_dimension=1, tiled=True)
    filter_share = lax.dynamic_slice_in_dim(filter_mask, layer_pos * (width // BS), width // BS, 1)
    product = summed_q.astype(jnp.bfloat16) * expand_mask(filter_share)

    pr_blocks = ring_gather(inner_rows(masked_p, groups, width, layer_pos), "row", nrow)
    p_inner = jnp.concatenate(pr_blocks, axis=0)
    p_inner = lax.dynamic_slice_in_dim(jnp.concatenate([p_inner, p_inner], 0), (nrow - row_me) % nrow * (groups * width), nrow * groups * width, 0)
    p_rows = lax.dynamic_slice_in_dim(jnp.concatenate([p_inner, p_inner], 0), col_me * width, ncol * width, 0)
    q_blocks = ring_gather(product, "col", ncol)
    partial_w = ring_dot(q_blocks, p_rows, width)
    weighted = lax.psum(partial_w, "layer").astype(jnp.bfloat16)
    return weighted


def solution(mesh):
    placed = (P("row", "col"), P("row", "col"), P("row", "col"), P("row", "col"), P("row", "col"))
    return jax.shard_map(
        local, mesh=mesh, in_specs=placed, out_specs=P("row", "col"), check_vma=False
    )
```
